32 devices in a mesh: fsdp: 8 (over y, x, core), dp: 4 (over z).
Axes of the slice: x: 2, y: 2, z: 4, core: 2. Of those that a mesh axis runs over, the one named last changes fastest.
Arguments:
- tokens: bfloat16 [131072, 1024], P(('fsdp', 'dp')), may hold values from -6 to 6
- cotangent: bfloat16 [131072, 1024], P(('fsdp', 'dp')), may hold values from -6 to 6
- lengths: int32 [256], P(('fsdp', 'dp')), may hold values from 8 to 2048, as said below
- selected: int32 [16384], P(('fsdp', 'dp')), may hold values from 0 to 4095, as said below
- attn_in: bfloat16 [1024, 3072], P('fsdp'), may hold values from -0.1875 to 0.1875
- attn_out: bfloat16 [1024, 1024], P('fsdp'), may hold values from -0.75 to 0.75
- mlp_in: bfloat16 [1024, 4096], P('fsdp'), may hold values from -0.1875 to 0.1875
- mlp_out: bfloat16 [4096, 1024], P('fsdp'), may hold values from -0.09375 to 0.09375
- norm_attn: bfloat16 [1024], P('fsdp'), may hold values from 0.5 to 1.5
- norm_mlp: bfloat16 [1024], P('fsdp'), may hold values from 0.5 to 1.5
- router: bfloat16 [1024], replicated, may hold values from -0.1875 to 0.1875
Outputs:
- output: bfloat16 [131072, 1024], P(('fsdp', 'dp'))
- grad_tokens: bfloat16 [131072, 1024], P(('fsdp', 'dp'))
- grad_attn_in: float32 [1024, 3072], P('fsdp')
- grad_attn_out: float32 [1024, 1024], P('fsdp')
- grad_mlp_in: float32 [1024, 4096], P('fsdp')
- grad_mlp_out: float32 [4096, 1024], P('fsdp')
- grad_norm_attn: float32 [1024], P('fsdp')
- grad_norm_mlp: float32 [1024], P('fsdp')
- grad_router: float32 [1024], replicated
The draws below stay inside these ranges and needn't reach their ends.
Inputs may be any that keep to these rules, and one draw needn't show every extreme that they name: `lengths`: each aligned block of 8 entries (one device's sequences, in order) holds multiples of 8 that sum to 4096; exactly one of them equals 2048. `selected`: each aligned block of 512 entries lists distinct positions within its device's 4096 tokens in ascending order; a sequence of length L has exactly L / 8 of its positions listed.
All inputs are finite; a program needn't handle non-finite values.
Results may differ from the reference program's by a relative error of at most 0.014.
Values may be sent and summed in bfloat16 or wider, within the bound.
No kernel may reach another device: no remote copies, remote signals or barrier semaphores. Data moves between devices by JAX's collectives and lax.ppermute only.
A program may use at most 192 MiB of HBM per device.

```python
import jax
import jax.numpy as jnp
from jax import lax

D = 1024
HEADS = 16
HEAD = 64
FF = 4096
TOK_DEV = 4096
SEQ_DEV = 8
K_DEV = 512
LONGEST = 2048
BLOCKS = 32
TOKENS = 131072


def block_lengths(key):
    rest_units = TOK_DEV // 16
    cut_key, slot_key = jax.random.split(key)
    cut_points = jnp.sort(jax.random.permutation(cut_key, rest_units - 1)[:SEQ_DEV - 2] + 1).astype(jnp.int32)
    bounds = jnp.concatenate([jnp.zeros((1,), jnp.int32), cut_points, jnp.full((1,), rest_units, jnp.int32)])
    part_sizes = bounds[1:] - bounds[:-1]
    long_slot = jax.random.randint(slot_key, (), 0, SEQ_DEV)
    slot_index = jnp.arange(SEQ_DEV, dtype=jnp.int32)
    source_slot = jnp.clip(slot_index - (slot_index > long_slot).astype(jnp.int32), 0, SEQ_DEV - 2)
    filled = jnp.where(slot_index == long_slot, LONGEST // 8, part_sizes[source_slot])
    return (8 * filled).astype(jnp.int32)


def block_routes(key, lengths):
    seq_ends = jnp.cumsum(lengths)
    starts = seq_ends - lengths
    positions = jnp.arange(TOK_DEV, dtype=jnp.int32)
    owner_seq = jnp.sum((positions[:, None] >= seq_ends[None, :]).astype(jnp.int32), axis=1)
    shuffled = jax.random.permutation(key, TOK_DEV).astype(jnp.int32)
    ordering = jnp.argsort(owner_seq * TOK_DEV + shuffled, stable=True).astype(jnp.int32)
    owner_sorted = owner_seq[ordering]
    rank_in_seq = positions - starts[owner_sorted]
    chosen = rank_in_seq < lengths[owner_sorted] // 8
    return jnp.sort(jnp.where(chosen, ordering, TOK_DEV))[:K_DEV].astype(jnp.int32)


def all_blocks(key):
    block_keys = jax.random.split(jax.random.fold_in(key, 7), BLOCKS)
    lengths = jax.vmap(block_lengths)(block_keys)
    route_keys = jax.random.split(jax.random.fold_in(key, 11), BLOCKS)
    routes = jax.vmap(block_routes)(route_keys, lengths)
    return (lengths, routes)


def draw_lengths(key, part):
    return all_blocks(key)[0].reshape(BLOCKS * SEQ_DEV)


def draw_selected(key, part):
    return all_blocks(key)[1].reshape(BLOCKS * K_DEV)


def block_scale(stream_key, shape, cuts, smallest, high):
    gain, own = 1.0, jax.random.fold_in(stream_key, 6)
    for dim, shards_of in cuts:
        draws = jnp.exp(jax.random.uniform(jax.random.fold_in(own, dim), (shards_of,), jnp.float32, smallest / len(cuts), high / len(cuts)))
        gain = gain * jnp.repeat(draws, shape[dim] // shards_of).reshape([-1 if axis == dim else 1 for axis in range(len(shape))])
    return gain


def scatter_about(rng, shape, scale, reach, cuts=(), kind=jnp.bfloat16):
    loudness = block_scale(rng, shape, cuts, -0.22, 0.18) if cuts else 1.0
    entries = jax.random.normal(rng, shape, jnp.float32) * scale * loudness
    return jnp.minimum(jnp.maximum(entries, -reach), reach).astype(kind)


def setup_inputs(seed: int = 0) -> dict:
    keys = jax.random.split(jax.random.key(seed), 12)
    tokens = scatter_about(keys[0], (TOKENS, D), 1.0, 6.0, ((0, 32),))
    cotangent = scatter_about(keys[1], (TOKENS, D), 1.0, 6.0, ((0, 32),))
    lengths = draw_lengths(jax.random.fold_in(keys[11], 71), 0)
    selected = draw_selected(jax.random.fold_in(keys[11], 71), 0)
    attn_in = scatter_about(keys[4], (D, 3 * D), D ** -0.5, 0.1875, ((0, 8),))
    attn_out = scatter_about(keys[5], (D, D), (D // 16) ** -0.5, 0.75, ((0, 8),))
    mlp_in = scatter_about(keys[6], (D, FF), D ** -0.5, 0.1875, ((0, 8),))
    mlp_out = scatter_about(keys[7], (FF, D), FF ** -0.5, 0.09375, ((0, 8),))
    norm_attn = jnp.clip(1.0 + 0.1 * jax.random.normal(keys[8], (D,), jnp.float32), 0.5, 1.5).astype(jnp.bfloat16)
    norm_mlp = jnp.clip(1.0 + 0.1 * jax.random.normal(keys[9], (D,), jnp.float32), 0.5, 1.5).astype(jnp.bfloat16)
    router = scatter_about(keys[10], (D,), D ** -0.5, 0.1875)
    return dict(tokens=tokens, cotangent=cotangent, lengths=lengths, selected=selected, attn_in=attn_in, attn_out=attn_out, mlp_in=mlp_in, mlp_out=mlp_out, norm_attn=norm_attn, norm_mlp=norm_mlp, router=router)


EPS = 1e-06
MASKED = -1e+30
HIGHEST_PRECISION = lax.Precision.HIGHEST

@jax.custom_vjp
def low(v):
    return lax.optimization_barrier(v.astype(jnp.bfloat16)).astype(jnp.float32)

@jax.custom_vjp
def low_back(v):
    return v

def low_keep(v):
    return (low(v), None)

def low_pass(kept, grad):
    return (grad,)

def back_keep(v):
    return (v, None)

def back_low(kept, grad):
    return (low(grad),)
low.defvjp(low_keep, low_pass)
low_back.defvjp(back_keep, back_low)

def rms_scale(values, gain_vec):
    return values * lax.rsqrt(lax.optimization_barrier(jnp.mean(values * values, axis=-1, keepdims=True)) + EPS) * gain_vec

def seq_mask(lengths, selected):
    seq_ends = jnp.cumsum(lengths)
    owner_seq = lax.optimization_barrier(jnp.sum((selected[:, None] >= seq_ends[None, :]).astype(jnp.int32), axis=1))
    return (owner_seq[:, None] == owner_seq[None, :]) & (selected[None, :] <= selected[:, None])

def attend(qkv, allowed):
    row_count = qkv.shape[0]
    query_heads = qkv[:, :D].reshape(row_count, HEADS, HEAD)
    key_heads = qkv[:, D:2 * D].reshape(row_count, HEADS, HEAD)
    value_heads = qkv[:, 2 * D:].reshape(row_count, HEADS, HEAD)
    scores = low_back(jnp.einsum('qhd,khd->hqk', query_heads, key_heads, precision=HIGHEST_PRECISION) * HEAD ** (-0.5))
    scores = jnp.where(allowed[None], scores, MASKED)
    probabilities = low(jax.nn.softmax(scores, axis=-1))
    attn_mix = jnp.einsum('hqk,khd->qhd', probabilities, value_heads, precision=HIGHEST_PRECISION).reshape(row_count, D)
    return low_back(low(attn_mix))

def one_block(weights, tokens, lengths, selected):
    attn_in, attn_out, mlp_in, mlp_out, norm_attn, norm_mlp, router = weights
    allowed = seq_mask(lengths, selected)
    routed = low_back(jnp.take(tokens, selected, axis=0))
    router_rate = jnp.dot(routed, router, precision=HIGHEST_PRECISION)
    normed = low(rms_scale(routed, norm_attn))
    qkv = low_back(low(jnp.dot(normed, attn_in, precision=HIGHEST_PRECISION)))
    attn_mix = attend(qkv, allowed)
    attended = low_back(jnp.dot(attn_mix, attn_out, precision=HIGHEST_PRECISION))
    middle = routed + attended
    normed_two = low(rms_scale(middle, norm_mlp))
    pre_gelu = low_back(jnp.dot(normed_two, mlp_in, precision=HIGHEST_PRECISION))
    active = low(jax.nn.gelu(pre_gelu))
    expanded = low_back(jnp.dot(active, mlp_out, precision=HIGHEST_PRECISION))
    branch = low(router_rate[:, None] * (attended + expanded))
    return tokens.at[selected].add(branch)

def layer_forward(weights, tokens, lengths, selected):
    blocks = tokens.reshape(BLOCKS, TOK_DEV, D)
    len_blocks = lengths.reshape(BLOCKS, SEQ_DEV)
    route_blocks = selected.reshape(BLOCKS, K_DEV)
    remat_block = jax.checkpoint(one_block)
    outputs = lax.map(lambda pieces: remat_block(weights, pieces[0], pieces[1], pieces[2]), (blocks, len_blocks, route_blocks))
    return outputs.reshape(TOKENS, D)

def reference(tokens, cotangent, lengths, selected, attn_in, attn_out, mlp_in, mlp_out, norm_attn, norm_mlp, router):
    weights = tuple((weight.astype(jnp.float32) for weight in (attn_in, attn_out, mlp_in, mlp_out, norm_attn, norm_mlp, router)))

    def forward(weights, tokens_float):
        return layer_forward(weights, tokens_float, lengths, selected)
    output, pullback = jax.vjp(forward, weights, tokens.astype(jnp.float32))
    grad_weights, grad_tokens = pullback(cotangent.astype(jnp.float32))
    return (output.astype(jnp.bfloat16), grad_tokens.astype(jnp.bfloat16), grad_weights[0], grad_weights[1], grad_weights[2], grad_weights[3], grad_weights[4], grad_weights[5], grad_weights[6])
```

```python
import numpy as np

import jax
import jax.numpy as jnp
from jax import lax
from jax.sharding import PartitionSpec as P

HEADS = 16
HEAD = 64


EPS = 1e-06
MASKED = -1e30


def rms_scale(values, gain_vec):
    return values * lax.rsqrt(jnp.mean(values * values, axis=-1, keepdims=True) + EPS) * gain_vec


def seq_mask(lengths, selected):
    seq_ends = jnp.cumsum(lengths)
    owner_seq = jnp.sum((selected[:, None] >= seq_ends[None, :]).astype(jnp.int32), axis=1)
    return (owner_seq[:, None] == owner_seq[None, :]) & (selected[None, :] <= selected[:, None])


def split_heads(matrix):
    return matrix.reshape(matrix.shape[0], HEADS, HEAD)


def masked_scores(query_heads, key_heads, allowed, score_scale):
    scores = (
        jnp.einsum("qhd,khd->hqk", query_heads, key_heads, preferred_element_type=jnp.float32)
        * score_scale
    )
    return jnp.where(allowed[None], scores, MASKED)


def plane_layout(mesh):
    devs = np.asarray(mesh.devices)
    if devs.ndim != 2 or devs.shape[0] != 8:
        return False
    try:
        for j in range(devs.shape[1]):
            for i in range(8):
                here = devs[i, j]
                mate = devs[i ^ 1, j]
                if tuple(mate.coords) != tuple(here.coords) or mate.core_on_chip == here.core_on_chip:
                    return False
                steps = []
                for bit in (2, 4):
                    other = devs[i ^ bit, j]
                    if other.core_on_chip != here.core_on_chip:
                        return False
                    diff = [abs(a - b) for a, b in zip(other.coords, here.coords)]
                    if sorted(diff) != [0] * (len(diff) - 1) + [1]:
                        return False
                    steps.append(diff.index(1))
                if steps[0] == steps[1]:
                    return False
    except AttributeError:
        return False
    return True


def swap_pairs(bit, size):
    return [(i, i ^ bit) for i in range(size)]


def plane_reduce(grad):
    rows, cols = grad.shape
    part = rows // 8
    half = part // 2
    me = lax.axis_index("fsdp")
    core = me % 2
    xi = (me // 2) % 2
    yi = me // 4
    blocks = grad.reshape(4, 2, part, cols)
    keep = lax.dynamic_index_in_dim(blocks, core, axis=1, keepdims=False)
    send = lax.dynamic_index_in_dim(blocks, 1 - core, axis=1, keepdims=False)
    got = lax.ppermute(send.astype(jnp.bfloat16), "fsdp", swap_pairs(1, 8))
    chip = keep + got.astype(jnp.float32)

    def pick(y, x):
        return lax.dynamic_index_in_dim(chip, y * 2 + x, axis=0, keepdims=False)

    own = pick(yi, xi)
    to_x = pick(yi, 1 - xi)
    to_y = pick(1 - yi, xi)
    to_d = pick(1 - yi, 1 - xi)
    first_x = lax.ppermute(
        jnp.stack([to_x[:half], to_d[:half]]).astype(jnp.bfloat16), "fsdp", swap_pairs(2, 8)
    ).astype(jnp.float32)
    first_y = lax.ppermute(
        jnp.stack([to_y[half:], to_d[half:]]).astype(jnp.bfloat16), "fsdp", swap_pairs(4, 8)
    ).astype(jnp.float32)
    own_a = own[:half] + first_x[0]
    pass_a = to_y[:half] + first_x[1]
    own_b = own[half:] + first_y[0]
    pass_b = to_x[half:] + first_y[1]
    second_y = lax.ppermute(pass_a.astype(jnp.bfloat16), "fsdp", swap_pairs(4, 8)).astype(jnp.float32)
    second_x = lax.ppermute(pass_b.astype(jnp.bfloat16), "fsdp", swap_pairs(2, 8)).astype(jnp.float32)
    shard = jnp.concatenate([own_a + second_y, own_b + second_x], axis=0)
    return lax.psum(shard.astype(jnp.bfloat16), "dp").astype(jnp.float32)


def plain_reduce(grad):
    shard = lax.psum_scatter(grad.astype(jnp.bfloat16), "fsdp", scatter_dimension=0, tiled=True)
    return lax.psum(shard, "dp").astype(jnp.float32)


def make_per_device(reduce_grad):
    def per_device(
        tokens,
        cotangent,
        lengths,
        selected,
        attn_in,
        attn_out,
        mlp_in,
        mlp_out,
        norm_attn,
        norm_mlp,
        router,
    ):
        model_width = tokens.shape[1]
        row_count = selected.shape[0]
        score_scale = HEAD ** (-0.5)
        w_qkv, gain_attn = (
            lax.all_gather(attn_in, "fsdp", axis=0, tiled=True),
            lax.all_gather(norm_attn, "fsdp", axis=0, tiled=True),
        )
        w_out = lax.all_gather(attn_out, "fsdp", axis=0, tiled=True)
        w_in, gain_mlp = (
            lax.all_gather(mlp_in, "fsdp", axis=0, tiled=True),
            lax.all_gather(norm_mlp, "fsdp", axis=0, tiled=True),
        )
        w_down = lax.all_gather(mlp_out, "fsdp", axis=0, tiled=True)
        gain_one = gain_attn.astype(jnp.float32)
        gain_two = gain_mlp.astype(jnp.float32)
        positions = lax.broadcasted_iota(jnp.int32, (row_count, tokens.shape[0]), 1)
        select = (selected[:, None] == positions).astype(jnp.bfloat16)
        routed = jnp.dot(select, tokens, preferred_element_type=jnp.float32)
        routed_low = routed.astype(jnp.bfloat16)
        router_rate = jnp.dot(routed_low, router, preferred_element_type=jnp.float32)
        allowed = seq_mask(lengths, selected)
        normed_float, norm_pull = jax.vjp(rms_scale, routed, gain_one)
        normed = normed_float.astype(jnp.bfloat16)
        qkv = jnp.dot(normed, w_qkv, preferred_element_type=jnp.float32).astype(jnp.bfloat16)
        query_heads = split_heads(qkv[:, :model_width])
        key_heads = split_heads(qkv[:, model_width : 2 * model_width])
        value_heads = split_heads(qkv[:, 2 * model_width :])
        scores = masked_scores(query_heads, key_heads, allowed, score_scale)
        highest = jnp.max(scores, axis=-1, keepdims=True)
        exponent = jnp.exp(scores - highest)
        row_total = jnp.sum(exponent, axis=-1, keepdims=True)
        probabilities = (exponent / row_total).astype(jnp.bfloat16)
        log_total = highest + jnp.log(row_total)
        attn_mix = jnp.einsum(
            "hqk,khd->qhd", probabilities, value_heads, preferred_element_type=jnp.float32
        )
        attn_mix = attn_mix.reshape(row_count, model_width).astype(jnp.bfloat16)
        attended = jnp.dot(attn_mix, w_out, preferred_element_type=jnp.float32)
        middle = routed + attended
        normed_two_float, middle_pull = jax.vjp(rms_scale, middle, gain_two)
        normed_two = normed_two_float.astype(jnp.bfloat16)
        pre_gelu = jnp.dot(normed_two, w_in, preferred_element_type=jnp.float32)
        active_float, gelu_pull = jax.vjp(jax.nn.gelu, pre_gelu)
        active = active_float.astype(jnp.bfloat16)
        expanded = jnp.dot(active, w_down, preferred_element_type=jnp.float32)
        update = attended + expanded
        branch = (router_rate[:, None] * update).astype(jnp.bfloat16)
        output = (
            tokens.astype(jnp.float32)
            + jnp.einsum("kt,kd->td", select, branch, preferred_element_type=jnp.float32)
        ).astype(jnp.bfloat16)
        cot_rows = jnp.dot(select, cotangent, preferred_element_type=jnp.float32)
        grad_rate = jnp.sum(cot_rows * update, axis=-1)
        grad_update = cot_rows * router_rate[:, None]
        grad_expanded = grad_update.astype(jnp.bfloat16)
        grad_down = jnp.einsum("kf,kd->fd", active, grad_expanded, preferred_element_type=jnp.float32)
        shard_down = reduce_grad(grad_down)
        grad_active = jnp.einsum(
            "kd,fd->kf", grad_expanded, w_down, preferred_element_type=jnp.float32
        )
        (grad_inner_float,) = gelu_pull(grad_active)
        grad_inner = grad_inner_float.astype(jnp.bfloat16)
        grad_up = jnp.einsum("kd,kf->df", normed_two, grad_inner, preferred_element_type=jnp.float32)
        shard_up = reduce_grad(grad_up)
        grad_normed_two = jnp.einsum(
            "kf,df->kd", grad_inner, w_in, preferred_element_type=jnp.float32
        )
        grad_middle, grad_gain_two = middle_pull(grad_normed_two)
        grad_attended = (grad_update + grad_middle).astype(jnp.bfloat16)
        grad_proj = jnp.einsum("ka,kd->ad", attn_mix, grad_attended, preferred_element_type=jnp.float32)
        shard_proj = reduce_grad(grad_proj)
        grad_mix = jnp.einsum(
            "kd,ad->ka", grad_attended, w_out, preferred_element_type=jnp.float32
        ).astype(jnp.bfloat16)
        grad_mix_heads = split_heads(grad_mix)
        scores_again = masked_scores(query_heads, key_heads, allowed, score_scale)
        prob_float = jnp.where(allowed[None], jnp.exp(scores_again - log_total), 0.0)
        grad_probs = jnp.einsum(
            "qhd,khd->hqk", grad_mix_heads, value_heads, preferred_element_type=jnp.float32
        )
        row_delta = jnp.sum(prob_float * grad_probs, axis=-1, keepdims=True)
        grad_scores = (prob_float * (grad_probs - row_delta)).astype(jnp.bfloat16)
        prob_low = prob_float.astype(jnp.bfloat16)
        grad_query = (
            jnp.einsum("hqk,khd->qhd", grad_scores, key_heads, preferred_element_type=jnp.float32)
            * score_scale
        )
        grad_key = (
            jnp.einsum("hqk,qhd->khd", grad_scores, query_heads, preferred_element_type=jnp.float32)
            * score_scale
        )
        grad_value = jnp.einsum(
            "hqk,qhd->khd", prob_low, grad_mix_heads, preferred_element_type=jnp.float32
        )
        grad_qkv = jnp.concatenate(
            [
                grad_query.reshape(row_count, model_width),
                grad_key.reshape(row_count, model_width),
                grad_value.reshape(row_count, model_width),
            ],
            axis=1,
        ).astype(jnp.bfloat16)
        grad_proj_in = jnp.einsum("kd,ke->de", normed, grad_qkv, preferred_element_type=jnp.float32)
        shard_qkv = reduce_grad(grad_proj_in)
        grad_normed = jnp.einsum("ke,de->kd", grad_qkv, w_qkv, preferred_element_type=jnp.float32)
        grad_routed_norm, grad_gain_one = norm_pull(grad_normed)
        grad_routed = (
            grad_routed_norm + grad_middle + grad_rate[:, None] * router.astype(jnp.float32)
        ).astype(jnp.bfloat16)
        grad_tokens = (
            cotangent.astype(jnp.float32)
            + jnp.einsum("kt,kd->td", select, grad_routed, preferred_element_type=jnp.float32)
        ).astype(jnp.bfloat16)
        router_local = jnp.dot(grad_rate, routed, precision=lax.Precision.HIGHEST)
        small = lax.psum(
            jnp.concatenate([grad_gain_one, grad_gain_two, router_local]), ("fsdp", "dp")
        )
        gain_part = grad_gain_one.shape[0] // lax.axis_size("fsdp")
        me = lax.axis_index("fsdp")
        shard_gain_one = lax.dynamic_slice_in_dim(small, me * gain_part, gain_part)
        shard_gain_two = lax.dynamic_slice_in_dim(
            small, grad_gain_one.shape[0] + me * gain_part, gain_part
        )
        grad_router = small[2 * grad_gain_one.shape[0] :]
        return (
            output,
            grad_tokens,
            shard_qkv,
            shard_proj,
            shard_up,
            shard_down,
            shard_gain_one,
            shard_gain_two,
            grad_router,
        )

    return per_device


def solution(mesh):
    placed = (
        P(("fsdp", "dp"), None),
        P(("fsdp", "dp"), None),
        P(("fsdp", "dp")),
        P(("fsdp", "dp")),
        P("fsdp", None),
        P("fsdp", None),
        P("fsdp", None),
        P("fsdp", None),
        P("fsdp"),
        P("fsdp"),
        P(),
    )
    reduce_grad = plane_reduce if plane_layout(mesh) else plain_reduce
    return jax.shard_map(
        make_per_device(reduce_grad),
        mesh=mesh,
        in_specs=placed,
        out_specs=(
            P(("fsdp", "dp"), None),
            P(("fsdp", "dp"), None),
            P("fsdp", None),
            P("fsdp", None),
            P("fsdp", None),
            P("fsdp", None),
            P("fsdp"),
            P("fsdp"),
            P(),
        ),
        check_vma=False,
    )
```
